512 devices in a mesh: dp: 16 (over z), owner: 32 (over x, y, core).
Axes of the slice: x: 4, y: 4, z: 16, core: 2. Of those that a mesh axis runs over, the one named last changes fastest.
Arguments:
- tokens: bfloat16 [65536, 8192], P(('dp', 'owner')), may hold values from -6 to 6
- residual: bfloat16 [65536, 8192], P(('dp', 'owner')), may hold values from -6 to 6
- token_adapter_index: int32 [65536, 1], P(('dp', 'owner')), may hold values from 0 to 31; in each aligned block of 128 rows (0 to 127, 128 to 255, ...) at most 6 rows name the same one
- adapter_down_weight: bfloat16 [32, 64, 8192], P('owner', None, 'dp'), may hold values from -0.0625 to 0.0625
- adapter_up_weight: bfloat16 [32, 64, 8192], P('owner', None, 'dp'), may hold values from -0.75 to 0.75
- down_moment_first: bfloat16 [32, 64, 8192], P('owner', None, 'dp'), may hold values from -270 to 270
- down_moment_second: bfloat16 [32, 64, 8192], P('owner', None, 'dp'), may hold values from 816 to 24576
- up_moment_first: bfloat16 [32, 64, 8192], P('owner', None, 'dp'), may hold values from -27.125 to 27.125
- up_moment_second: bfloat16 [32, 64, 8192], P('owner', None, 'dp'), may hold values from 6.125 to 204
Outputs:
- down_update: float32 [32, 64, 8192], P('owner', None, 'dp')
- up_update: float32 [32, 64, 8192], P('owner', None, 'dp')
- token_loss: float32 [65536], P(('dp', 'owner'))
The draws below stay inside these ranges and needn't reach their ends.
Inputs may be any that keep to these rules, and one draw needn't show every extreme that they name: `token_adapter_index`: of the 128 rows of one device, at most 6 name one adapter, and in some devices one adapter is named by exactly 6.
All inputs are finite; a program needn't handle non-finite values.
Results may differ from the reference program's by a relative error of at most 0.0091.
Values may be sent and summed in bfloat16 or wider, within the bound.
No kernel may reach another device: no remote copies, remote signals or barrier semaphores. Data moves between devices by JAX's collectives and lax.ppermute only.
A program may use at most 128 MiB of HBM per device.

```python
import math
import jax
import jax.numpy as jnp
import numpy as np
from jax import lax

MODEL_DIM = 8192
ADAPTER_RANK = 64
TOK_DEV = 128
ADAPTER_COUNT = 32
TOKENS = 65536
MOST = 6
TENANT_ROWS = 2048
N_DP = 16
N_OWNER = 32


def level_of(rng, extent, split, least, top_value):
    level, own = 1.0, jax.random.fold_in(rng, 6)
    for axis_at, shards_of in split:
        steps = jnp.exp(jax.random.uniform(jax.random.fold_in(own, axis_at), (shards_of,), jnp.float32, least / len(split), top_value / len(split)))
        level = level * jnp.repeat(steps, extent[axis_at] // shards_of).reshape([-1 if axis == axis_at else 1 for axis in range(len(extent))])
    return level


def routed_block(rng, own, number, rows, amount, top, limit, lean):
    order = jax.random.permutation(rng, amount)
    crowded, usual = shares(amount, rows * top, limit, lean, True), shares(amount, rows * top, limit, lean, False)
    places = jnp.arange(amount)

    def named(sizes, turn):
        used = int((sizes > 0).sum())
        fixed = max(1, used // 4)
        shifted = fixed + (places - fixed + turn * (used - fixed)) % max(1, amount - fixed)
        return jnp.zeros((amount,), jnp.int32).at[order[jnp.where(places < fixed, places, shifted)]].set(jnp.asarray(sizes, jnp.int32))

    sizes = jnp.where(number % 4 == 0, named(crowded, number // 4), named(usual, number - number // 4 - 1))
    mixed = jax.random.permutation(jax.random.fold_in(own, 3), amount)
    giver, sink = mixed[0:amount // 2 * 2:2], mixed[1:amount // 2 * 2:2]
    room = jnp.minimum(sizes[giver] - 1, limit - sizes[sink]) // 2
    room = jnp.where((giver == order[0]) | (sink == order[0]) | (sizes[sink] == 0), 0, jnp.maximum(room, 0))
    shifted = jax.random.randint(jax.random.fold_in(own, 4), (amount // 2,), 0, 1 << 20) % (room + 1)
    sizes = sizes.at[giver].add(-shifted).at[sink].add(shifted)
    members = jnp.searchsorted(jnp.cumsum(sizes), jnp.arange(rows * top), side="right").astype(jnp.int32)
    table = members.reshape(top, rows).T
    table = table[jax.random.permutation(jax.random.fold_in(own, 1), rows)]
    turn = jax.random.randint(jax.random.fold_in(own, 2), (rows, 1), 0, top)
    return jnp.take_along_axis(table, (jnp.arange(top)[None, :] + turn) % top, axis=1)


def shares(amount, total, most, skew, full):
    weights = [(1 << 20) // math.isqrt(grade ** skew) + 1 for grade in range(1, amount + 1)]
    largest = most if full else min(most, max(-(-total // amount), total * weights[0] // sum(weights)))
    least = 1 if total - largest >= amount - 1 else 0
    given, spare = [largest] + [least] * (amount - 1), total - largest - least * (amount - 1)
    while spare > 0:
        candidates = [i for i in range(1, amount) if given[i] < largest] or [i for i in range(1, amount) if given[i] < most]
        pool, left = sum([weights[i] for i in candidates]), spare
        for i in candidates:
            extra = min(most - given[i], max(1, left * weights[i] // pool), spare)
            given[i] = given[i] + extra
            spare = spare - extra
    return np.array(given)


def scatter_about(own_key, dims, spread, limit, split=(), held_as=jnp.bfloat16):
    gain = level_of(own_key, dims, split, -0.22, 0.18) if split else 1.0
    result = jax.random.normal(own_key, dims, jnp.float32) * spread * gain
    return jnp.minimum(jnp.maximum(result, -limit), limit).astype(held_as)


def setup_inputs(seed: int = 0) -> dict:
    key_list = jax.random.split(jax.random.key(seed), 10)
    tokens = scatter_about(key_list[0], (TOKENS, MODEL_DIM), 1.0, 6.0, ((0, 512),))
    residual = scatter_about(key_list[1], (TOKENS, MODEL_DIM), 1.0, 6.0, ((0, 512),))
    token_adapter_index_keys = jax.random.split(jax.random.fold_in(key_list[2], 1), TOKENS // TOK_DEV)
    token_adapter_index_turns = jax.random.permutation(jax.random.fold_in(key_list[2], 3), TOKENS // TOK_DEV)
    token_adapter_index = jax.vmap(lambda own, number: routed_block(jax.random.fold_in(key_list[2], 2), own, number, TOK_DEV, ADAPTER_COUNT, 1, MOST, 2))(token_adapter_index_keys, token_adapter_index_turns).reshape((TOKENS, 1))
    adapter_down_weight = scatter_about(key_list[3], (ADAPTER_COUNT, ADAPTER_RANK, MODEL_DIM), MODEL_DIM ** -0.5, 0.0625, ((0, 32), (2, 16)))
    adapter_up_weight = scatter_about(key_list[4], (ADAPTER_COUNT, ADAPTER_RANK, MODEL_DIM), ADAPTER_RANK ** -0.5, 0.75, ((0, 32), (2, 16)))
    down_moment_first = scatter_about(key_list[5], (ADAPTER_COUNT, ADAPTER_RANK, MODEL_DIM), (1.2 * TENANT_ROWS ** 0.5), 270.0, ((0, 32), (2, 16)))
    down_moment_second = jnp.clip(jnp.exp(math.log(24576.0) - 3.4051113 * jax.random.uniform(key_list[6], (ADAPTER_COUNT, ADAPTER_RANK, MODEL_DIM), jnp.float32) ** level_of(key_list[6], (ADAPTER_COUNT, ADAPTER_RANK, MODEL_DIM), ((0, 32), (2, 16)), -0.2, 0.2)), 816.0, 24576.0).astype(jnp.bfloat16)
    up_moment_first = scatter_about(key_list[7], (ADAPTER_COUNT, ADAPTER_RANK, MODEL_DIM), (0.1 * TENANT_ROWS ** 0.5), 27.125, ((0, 32), (2, 16)))
    up_moment_second = jnp.clip(jnp.exp(math.log(204.0) - 3.5057412 * jax.random.uniform(key_list[8], (ADAPTER_COUNT, ADAPTER_RANK, MODEL_DIM), jnp.float32) ** level_of(key_list[8], (ADAPTER_COUNT, ADAPTER_RANK, MODEL_DIM), ((0, 32), (2, 16)), -0.2, 0.2)), 6.125, 204.0).astype(jnp.bfloat16)
    return dict(tokens=tokens, residual=residual, token_adapter_index=token_adapter_index, adapter_down_weight=adapter_down_weight, adapter_up_weight=adapter_up_weight, down_moment_first=down_moment_first, down_moment_second=down_moment_second, up_moment_first=up_moment_first, up_moment_second=up_moment_second)


adapter_scale = 0.5
adam_eps = 1e-08

def adam_update(grad, first, second):
    first_new = 0.9 * first.astype(jnp.float32) + 0.1 * grad
    second_new = 0.95 * second.astype(jnp.float32) + 0.05 * grad * grad
    return first_new / (jnp.sqrt(second_new) + adam_eps)

def reference(tokens, residual, token_adapter_index, adapter_down_weight, adapter_up_weight, down_moment_first, down_moment_second, up_moment_first, up_moment_second):
    route_ids = token_adapter_index[:, 0]
    slots = N_DP * N_OWNER * MOST

    def per_adapter(adapter_slot):
        positions = jnp.nonzero(route_ids == adapter_slot, size=slots, fill_value=TOKENS)[0].astype(jnp.int32)
        present = positions < TOKENS
        clipped = jnp.minimum(positions, TOKENS - 1)
        row_block = jnp.where(present[:, None], tokens[clipped], jnp.zeros((), tokens.dtype))
        residual_row_block = jnp.where(present[:, None], residual[clipped].astype(jnp.float32), jnp.zeros((), jnp.float32))
        down_row_block = adapter_down_weight[adapter_slot]
        up_row_block = adapter_up_weight[adapter_slot]
        hidden_state = lax.dot_general(row_block, down_row_block, (((1,), (1,)), ((), ())), preferred_element_type=jnp.float32).astype(jnp.bfloat16)
        adapter_output = (adapter_scale * jnp.dot(hidden_state, up_row_block, preferred_element_type=jnp.float32)).astype(jnp.bfloat16)
        shifted_index = residual_row_block + adapter_output.astype(jnp.float32)
        row_loss = lax.optimization_barrier(jnp.mean(0.5 * shifted_index * shifted_index, axis=1))
        output_gradient = shifted_index.astype(jnp.bfloat16)
        up_gradient = adapter_scale * lax.dot_general(hidden_state, output_gradient, (((0,), (0,)), ((), ())), preferred_element_type=jnp.float32)
        hidden_gradient = (adapter_scale * lax.dot_general(output_gradient, up_row_block, (((1,), (1,)), ((), ())), preferred_element_type=jnp.float32)).astype(jnp.bfloat16)
        down_grad = lax.dot_general(hidden_gradient, row_block, (((0,), (0,)), ((), ())), preferred_element_type=jnp.float32)
        return (down_grad, up_gradient, row_loss, positions)
    down_grad, up_gradient, row_loss, positions = lax.map(per_adapter, jnp.arange(ADAPTER_COUNT, dtype=jnp.int32))
    token_loss = jnp.zeros((TOKENS,), jnp.float32).at[positions.reshape(-1)].set(row_loss.reshape(-1), mode='drop')
    down_update = adam_update(down_grad, down_moment_first, down_moment_second)
    up_update = adam_update(up_gradient, up_moment_first, up_moment_second)
    return (down_update, up_update, token_loss)
```

```python
import jax
import jax.numpy as jnp
from jax import lax
from jax.sharding import PartitionSpec as P

adapter_scale = 0.5
adam_eps = 1e-08


def adam_update(grad, first, second):
    first_new = 0.9 * first.astype(jnp.float32) + 0.1 * grad
    second_new = 0.95 * second.astype(jnp.float32) + 0.05 * grad * grad
    return first_new / (jnp.sqrt(second_new) + adam_eps)


def body(
    tokens,
    residual,
    token_adapter_index,
    adapter_down_weight,
    adapter_up_weight,
    down_moment_first,
    down_moment_second,
    up_moment_first,
    up_moment_second,
):
    owner_count = lax.axis_size("owner")
    tok_rows = tokens.shape[0]
    width = tokens.shape[1]
    rank = adapter_down_weight.shape[1]
    slot_capacity = max(2, 3 * tok_rows // (2 * owner_count))
    slots = owner_count * slot_capacity
    route_ids = token_adapter_index[:, 0]
    member = (route_ids[:, None] == jnp.arange(owner_count, dtype=jnp.int32)[None, :]).astype(
        jnp.int32
    )
    before = jnp.cumsum(member, axis=0) - member
    within = jnp.sum(before * member, axis=1)
    target = route_ids * slot_capacity + within
    dispatch = (jnp.arange(slots, dtype=jnp.int32)[:, None] == target[None, :]).astype(
        jnp.bfloat16
    )

    both_weights = jnp.concatenate([adapter_down_weight[0], adapter_up_weight[0]], axis=0)
    both_full = lax.all_gather(both_weights, "dp", axis=1, tiled=True)
    down_full = both_full[:rank]
    up_full = both_full[rank:]

    rows = jnp.concatenate([tokens, residual], axis=1)
    placed = jnp.dot(dispatch, rows, preferred_element_type=jnp.float32).astype(jnp.bfloat16)
    arrived_both = lax.all_to_all(
        placed.reshape(owner_count, slot_capacity, 2 * width),
        "owner",
        split_axis=0,
        concat_axis=0,
        tiled=True,
    ).reshape(slots, 2 * width)
    arrived = arrived_both[:, :width]
    arrived_residual = arrived_both[:, width:]

    hidden_state = lax.dot_general(
        arrived, down_full, (((1,), (1,)), ((), ())), preferred_element_type=jnp.float32
    ).astype(jnp.bfloat16)
    adapter_output = (
        adapter_scale * jnp.dot(hidden_state, up_full, preferred_element_type=jnp.float32)
    ).astype(jnp.bfloat16)
    shifted = arrived_residual.astype(jnp.float32) + adapter_output.astype(jnp.float32)
    slot_loss = jnp.mean(0.5 * shifted * shifted, axis=1)
    output_gradient = shifted.astype(jnp.bfloat16)
    up_gradient = adapter_scale * lax.dot_general(
        hidden_state, output_gradient, (((0,), (0,)), ((), ())), preferred_element_type=jnp.float32
    )
    hidden_gradient = (
        adapter_scale
        * lax.dot_general(
            output_gradient,
            up_full,
            (((1,), (1,)), ((), ())),
            preferred_element_type=jnp.float32,
        )
    ).astype(jnp.bfloat16)
    down_grad = lax.dot_general(
        hidden_gradient, arrived, (((0,), (0,)), ((), ())), preferred_element_type=jnp.float32
    )

    both_grads = jnp.concatenate([down_grad, up_gradient], axis=0)
    summed = lax.psum_scatter(both_grads, "dp", scatter_dimension=1, tiled=True)
    down_share = summed[:rank]
    up_share = summed[rank:]
    down_update = adam_update(down_share, down_moment_first[0], down_moment_second[0])
    up_update = adam_update(up_share, up_moment_first[0], up_moment_second[0])

    returned_loss = lax.all_to_all(
        slot_loss.reshape(owner_count, slot_capacity),
        "owner",
        split_axis=0,
        concat_axis=0,
        tiled=True,
    ).reshape(slots)
    token_loss = jnp.take(returned_loss, target, axis=0)
    return (down_update[None], up_update[None], token_loss)


def solution(mesh):
    return jax.shard_map(
        body,
        mesh=mesh,
        in_specs=(
            P(("dp", "owner"), None),
            P(("dp", "owner"), None),
            P(("dp", "owner"), None),
            P("owner", None, "dp"),
            P("owner", None, "dp"),
            P("owner", None, "dp"),
            P("owner", None, "dp"),
            P("owner", None, "dp"),
            P("owner", None, "dp"),
        ),
        out_specs=(P("owner", None, "dp"), P("owner", None, "dp"), P(("dp", "owner"))),
        check_vma=False,
    )
```

```python
import jax
import jax.numpy as jnp
from jax import lax
from jax.sharding import PartitionSpec as P

adapter_scale = 0.5
adam_eps = 1e-08


def adam_update(grad, first, second):
    first_new = 0.9 * first.astype(jnp.float32) + 0.1 * grad
    second_new = 0.95 * second.astype(jnp.float32) + 0.05 * grad * grad
    return first_new / (jnp.sqrt(second_new) + adam_eps)


def body(
    tokens,
    residual,
    token_adapter_index,
    adapter_down_weight,
    adapter_up_weight,
    down_moment_first,
    down_moment_second,
    up_moment_first,
    up_moment_second,
):
    owner_count = lax.axis_size("owner")
    tok_rows = tokens.shape[0]
    width = tokens.shape[1]
    rank = adapter_down_weight.shape[1]
    slot_capacity = max(2, 3 * tok_rows // (2 * owner_count))
    slots = owner_count * slot_capacity
    route_ids = token_adapter_index[:, 0]
    member = (route_ids[:, None] == jnp.arange(owner_count, dtype=jnp.int32)[None, :]).astype(
        jnp.int32
    )
    before = jnp.cumsum(member, axis=0) - member
    within = jnp.sum(before * member, axis=1)
    target = route_ids * slot_capacity + within
    dispatch = (jnp.arange(slots, dtype=jnp.int32)[:, None] == target[None, :]).astype(
        jnp.bfloat16
    )

    pieces = lax.axis_size("dp")
    piece = width // pieces
    valid = jnp.sum(dispatch, axis=1) > 0
    source = jnp.argmax(dispatch, axis=1)

    both_weights = jnp.concatenate([adapter_down_weight[0], adapter_up_weight[0]], axis=0)
    both_split = lax.all_gather(both_weights, "dp", axis=0, tiled=False)
    down_full = both_split[:, :rank]
    up_full = both_split[:, rank:]

    def place(row_block):
        split_rows = row_block.reshape(tok_rows, pieces, piece)
        picked = jnp.where(valid[:, None, None], split_rows[source], jnp.zeros((), row_block.dtype))
        return picked.reshape(owner_count, slot_capacity * pieces, piece)

    placed = jnp.concatenate([place(tokens), place(residual)], axis=1)
    arrived_both = lax.all_to_all(placed, "owner", split_axis=0, concat_axis=0, tiled=True)
    half = slot_capacity * pieces
    arrived = arrived_both[:, :half].reshape(slots, pieces, piece)
    arrived_residual = arrived_both[:, half:].reshape(slots, pieces, piece)

    hidden_state = jnp.einsum(
        "tkc,krc->tr", arrived, down_full, preferred_element_type=jnp.float32
    ).astype(jnp.bfloat16)
    adapter_output = (
        adapter_scale
        * jnp.einsum("tr,krc->tkc", hidden_state, up_full, preferred_element_type=jnp.float32)
    ).astype(jnp.bfloat16)
    shifted = arrived_residual.astype(jnp.float32) + adapter_output.astype(jnp.float32)
    slot_loss = jnp.mean(0.5 * shifted * shifted, axis=(1, 2))
    output_gradient = shifted.astype(jnp.bfloat16)
    up_gradient = adapter_scale * jnp.einsum(
        "tr,tkc->krc", hidden_state, output_gradient, preferred_element_type=jnp.float32
    )
    hidden_gradient = (
        adapter_scale
        * jnp.einsum("tkc,krc->tr", output_gradient, up_full, preferred_element_type=jnp.float32)
    ).astype(jnp.bfloat16)
    down_grad = jnp.einsum(
        "tr,tkc->krc", hidden_gradient, arrived, preferred_element_type=jnp.float32
    )

    both_grads = jnp.concatenate([down_grad, up_gradient], axis=1)
    summed = lax.psum_scatter(both_grads, "dp", scatter_dimension=0, tiled=False)
    down_share = summed[:rank]
    up_share = summed[rank:]
    down_update = adam_update(down_share, down_moment_first[0], down_moment_second[0])
    up_update = adam_update(up_share, up_moment_first[0], up_moment_second[0])

    returned_loss = lax.all_to_all(
        slot_loss.reshape(owner_count, slot_capacity),
        "owner",
        split_axis=0,
        concat_axis=0,
        tiled=True,
    ).reshape(slots)
    token_loss = jnp.take(returned_loss, target, axis=0)
    return (down_update[None], up_update[None], token_loss)


def solution(mesh):
    return jax.shard_map(
        body,
        mesh=mesh,
        in_specs=(
            P(("dp", "owner"), None),
            P(("dp", "owner"), None),
            P(("dp", "owner"), None),
            P("owner", None, "dp"),
            P("owner", None, "dp"),
            P("owner", None, "dp"),
            P("owner", None, "dp"),
            P("owner", None, "dp"),
            P("owner", None, "dp"),
        ),
        out_specs=(P("owner", None, "dp"), P("owner", None, "dp"), P(("dp", "owner"))),
        check_vma=False,
    )
```

```python
import jax
import jax.numpy as jnp
from jax import lax
from jax.sharding import PartitionSpec as P

adapter_scale = 0.5
adam_eps = 1e-08


def adam_update(grad, first, second):
    first_new = 0.9 * first.astype(jnp.float32) + 0.1 * grad
    second_new = 0.95 * second.astype(jnp.float32) + 0.05 * grad * grad
    return first_new / (jnp.sqrt(second_new) + adam_eps)


def body(
    tokens,
    residual,
    token_adapter_index,
    adapter_down_weight,
    adapter_up_weight,
    down_moment_first,
    down_moment_second,
    up_moment_first,
    up_moment_second,
):
    owner_count = lax.axis_size("owner")
    tok_rows = tokens.shape[0]
    width = tokens.shape[1]
    rank = adapter_down_weight.shape[1]
    slot_capacity = max(2, 3 * tok_rows // (2 * owner_count))
    slots = owner_count * slot_capacity
    route_ids = token_adapter_index[:, 0]
    member = (route_ids[:, None] == jnp.arange(owner_count, dtype=jnp.int32)[None, :]).astype(
        jnp.int32
    )
    before = jnp.cumsum(member, axis=0) - member
    within = jnp.sum(before * member, axis=1)
    target = route_ids * slot_capacity + within
    dispatch = (jnp.arange(slots, dtype=jnp.int32)[:, None] == target[None, :]).astype(
        jnp.bfloat16
    )

    pieces = lax.axis_size("dp")
    piece = width // pieces
    valid = jnp.sum(dispatch, axis=1) > 0
    source = jnp.argmax(dispatch, axis=1)

    both_weights = jnp.concatenate([adapter_down_weight[0], adapter_up_weight[0]], axis=0)
    both_full = lax.all_gather(both_weights, "dp", axis=1, tiled=True)
    down_full = both_full[:rank]
    up_full = both_full[rank:]

    def place(row_block):
        split_rows = row_block.reshape(tok_rows, pieces, piece)
        picked = jnp.where(valid[:, None, None], split_rows[source], jnp.zeros((), row_block.dtype))
        return picked.reshape(owner_count, slot_capacity * pieces, piece)

    placed = jnp.concatenate([place(tokens), place(residual)], axis=1)
    arrived_both = lax.all_to_all(placed, "owner", split_axis=0, concat_axis=0, tiled=True)
    half = slot_capacity * pieces
    arrived = arrived_both[:, :half].reshape(slots, width)
    arrived_residual = arrived_both[:, half:].reshape(slots, width)

    hidden_state = lax.dot_general(
        arrived, down_full, (((1,), (1,)), ((), ())), preferred_element_type=jnp.float32
    ).astype(jnp.bfloat16)
    adapter_output = (
        adapter_scale * jnp.dot(hidden_state, up_full, preferred_element_type=jnp.float32)
    ).astype(jnp.bfloat16)
    shifted = arrived_residual.astype(jnp.float32) + adapter_output.astype(jnp.float32)
    slot_loss = jnp.mean(0.5 * shifted * shifted, axis=1)
    output_gradient = shifted.astype(jnp.bfloat16)
    up_gradient = adapter_scale * lax.dot_general(
        hidden_state, output_gradient, (((0,), (0,)), ((), ())), preferred_element_type=jnp.float32
    )
    hidden_gradient = (
        adapter_scale
        * lax.dot_general(
            output_gradient,
            up_full,
            (((1,), (1,)), ((), ())),
            preferred_element_type=jnp.float32,
        )
    ).astype(jnp.bfloat16)
    down_grad = lax.dot_general(
        hidden_gradient, arrived, (((0,), (0,)), ((), ())), preferred_element_type=jnp.float32
    )

    both_grads = jnp.concatenate([down_grad, up_gradient], axis=0)
    summed = lax.psum_scatter(both_grads, "dp", scatter_dimension=1, tiled=True)
    down_share = summed[:rank]
    up_share = summed[rank:]
    down_update = adam_update(down_share, down_moment_first[0], down_moment_second[0])
    up_update = adam_update(up_share, up_moment_first[0], up_moment_second[0])

    returned_loss = lax.all_to_all(
        slot_loss.reshape(owner_count, slot_capacity),
        "owner",
        split_axis=0,
        concat_axis=0,
        tiled=True,
    ).reshape(slots)
    token_loss = jnp.take(returned_loss, target, axis=0)
    return (down_update[None], up_update[None], token_loss)


def solution(mesh):
    return jax.shard_map(
        body,
        mesh=mesh,
        in_specs=(
            P(("dp", "owner"), None),
            P(("dp", "owner"), None),
            P(("dp", "owner"), None),
            P("owner", None, "dp"),
            P("owner", None, "dp"),
            P("owner", None, "dp"),
            P("owner", None, "dp"),
            P("owner", None, "dp"),
            P("owner", None, "dp"),
        ),
        out_specs=(P("owner", None, "dp"), P("owner", None, "dp"), P(("dp", "owner"))),
        check_vma=False,
    )
```

```python
import jax
import jax.numpy as jnp
from jax import lax
from jax.sharding import PartitionSpec as P

adapter_scale = 0.5
adam_eps = 1e-08


def adam_update(grad, first, second):
    first_new = 0.9 * first.astype(jnp.float32) + 0.1 * grad
    second_new = 0.95 * second.astype(jnp.float32) + 0.05 * grad * grad
    return first_new / (jnp.sqrt(second_new) + adam_eps)


def body(
    tokens,
    residual,
    token_adapter_index,
    adapter_down_weight,
    adapter_up_weight,
    down_moment_first,
    down_moment_second,
    up_moment_first,
    up_moment_second,
):
    owner_count = lax.axis_size("owner")
    tok_rows = tokens.shape[0]
    width = tokens.shape[1]
    rank = adapter_down_weight.shape[1]
    slot_capacity = max(2, 3 * tok_rows // (2 * owner_count))
    slots = owner_count * slot_capacity
    route_ids = token_adapter_index[:, 0]
    member = (route_ids[:, None] == jnp.arange(owner_count, dtype=jnp.int32)[None, :]).astype(
        jnp.int32
    )
    before = jnp.cumsum(member, axis=0) - member
    within = jnp.sum(before * member, axis=1)
    target = route_ids * slot_capacity + within
    dispatch = (jnp.arange(slots, dtype=jnp.int32)[:, None] == target[None, :]).astype(
        jnp.bfloat16
    )

    pieces = lax.axis_size("dp")
    piece = width // pieces
    valid = jnp.sum(dispatch, axis=1) > 0
    source = jnp.argmax(dispatch, axis=1)

    both_weights = jnp.concatenate([adapter_down_weight[0], adapter_up_weight[0]], axis=0)
    both_full = lax.all_gather(both_weights, "dp", axis=1, tiled=True)
    down_full = both_full[:rank]
    up_full = both_full[rank:]

    def place(row_block):
        split_rows = row_block.reshape(tok_rows, pieces, piece)
        picked = jnp.where(valid[:, None, None], split_rows[source], jnp.zeros((), row_block.dtype))
        return picked.reshape(owner_count, slot_capacity * pieces, piece)

    def send(row_block):
        return lax.all_to_all(place(row_block), "owner", split_axis=0, concat_axis=0, tiled=True)

    arrived = send(tokens).reshape(slots, width)
    arrived_residual = lax.optimization_barrier(send(residual).reshape(slots, width))

    hidden_state = lax.dot_general(
        arrived, down_full, (((1,), (1,)), ((), ())), preferred_element_type=jnp.float32
    ).astype(jnp.bfloat16)
    adapter_output = (
        adapter_scale * jnp.dot(hidden_state, up_full, preferred_element_type=jnp.float32)
    ).astype(jnp.bfloat16)
    shifted = arrived_residual.astype(jnp.float32) + adapter_output.astype(jnp.float32)
    slot_loss = jnp.mean(0.5 * shifted * shifted, axis=1)
    output_gradient = shifted.astype(jnp.bfloat16)
    up_gradient = adapter_scale * lax.dot_general(
        hidden_state, output_gradient, (((0,), (0,)), ((), ())), preferred_element_type=jnp.float32
    )
    hidden_gradient = (
        adapter_scale
        * lax.dot_general(
            output_gradient,
            up_full,
            (((1,), (1,)), ((), ())),
            preferred_element_type=jnp.float32,
        )
    ).astype(jnp.bfloat16)
    down_grad = lax.dot_general(
        hidden_gradient, arrived, (((0,), (0,)), ((), ())), preferred_element_type=jnp.float32
    )

    both_grads = jnp.concatenate([down_grad, up_gradient], axis=0)
    summed = lax.psum_scatter(both_grads, "dp", scatter_dimension=1, tiled=True)
    down_share = summed[:rank]
    up_share = summed[rank:]
    down_update = adam_update(down_share, down_moment_first[0], down_moment_second[0])
    up_update = adam_update(up_share, up_moment_first[0], up_moment_second[0])

    returned_loss = lax.all_to_all(
        slot_loss.reshape(owner_count, slot_capacity),
        "owner",
        split_axis=0,
        concat_axis=0,
        tiled=True,
    ).reshape(slots)
    token_loss = jnp.take(returned_loss, target, axis=0)
    return (down_update[None], up_update[None], token_loss)


def solution(mesh):
    return jax.shard_map(
        body,
        mesh=mesh,
        in_specs=(
            P(("dp", "owner"), None),
            P(("dp", "owner"), None),
            P(("dp", "owner"), None),
            P("owner", None, "dp"),
            P("owner", None, "dp"),
            P("owner", None, "dp"),
            P("owner", None, "dp"),
            P("owner", None, "dp"),
            P("owner", None, "dp"),
        ),
        out_specs=(P("owner", None, "dp"), P("owner", None, "dp"), P(("dp", "owner"))),
        check_vma=False,
    )
```

```python
import jax
import jax.numpy as jnp
from jax import lax
from jax.sharding import PartitionSpec as P

adapter_scale = 0.5
adam_eps = 1e-08


def adam_update(grad, first, second):
    first_new = 0.9 * first.astype(jnp.float32) + 0.1 * grad
    second_new = 0.95 * second.astype(jnp.float32) + 0.05 * grad * grad
    return first_new / (jnp.sqrt(second_new) + adam_eps)


def body(
    tokens,
    residual,
    token_adapter_index,
    adapter_down_weight,
    adapter_up_weight,
    down_moment_first,
    down_moment_second,
    up_moment_first,
    up_moment_second,
):
    owner_count = lax.axis_size("owner")
    tok_rows = tokens.shape[0]
    width = tokens.shape[1]
    rank = adapter_down_weight.shape[1]
    slot_capacity = max(2, 3 * tok_rows // (2 * owner_count))
    slots = owner_count * slot_capacity
    route_ids = token_adapter_index[:, 0]
    member = (route_ids[:, None] == jnp.arange(owner_count, dtype=jnp.int32)[None, :]).astype(
        jnp.int32
    )
    before = jnp.cumsum(member, axis=0) - member
    within = jnp.sum(before * member, axis=1)
    target = route_ids * slot_capacity + within
    dispatch = (jnp.arange(slots, dtype=jnp.int32)[:, None] == target[None, :]).astype(
        jnp.bfloat16
    )

    pieces = lax.axis_size("dp")
    piece = width // pieces
    valid = jnp.sum(dispatch, axis=1) > 0
    source = jnp.argmax(dispatch, axis=1)

    both_weights = jnp.concatenate([adapter_down_weight[0], adapter_up_weight[0]], axis=0)
    both_full = lax.all_gather(both_weights, "dp", axis=1, tiled=True)
    down_full = both_full[:rank]
    up_full = both_full[rank:]

    def place(row_block):
        split_rows = row_block.reshape(tok_rows, pieces, piece)
        picked = jnp.where(valid[:, None, None], split_rows[source], jnp.zeros((), row_block.dtype))
        return picked.reshape(owner_count, slot_capacity * pieces, piece)

    def send(row_block):
        return lax.all_to_all(place(row_block), "owner", split_axis=0, concat_axis=0, tiled=True)

    arrived_tokens = send(tokens)
    placed_residual, arrived_tokens = lax.optimization_barrier((place(residual), arrived_tokens))
    arrived = arrived_tokens.reshape(slots, width)
    arrived_residual = lax.all_to_all(
        placed_residual, "owner", split_axis=0, concat_axis=0, tiled=True
    )
    arrived_residual = lax.optimization_barrier(arrived_residual.reshape(slots, width))

    hidden_state = lax.dot_general(
        arrived, down_full, (((1,), (1,)), ((), ())), preferred_element_type=jnp.float32
    ).astype(jnp.bfloat16)
    adapter_output = (
        adapter_scale * jnp.dot(hidden_state, up_full, preferred_element_type=jnp.float32)
    ).astype(jnp.bfloat16)
    shifted = arrived_residual.astype(jnp.float32) + adapter_output.astype(jnp.float32)
    slot_loss = jnp.mean(0.5 * shifted * shifted, axis=1)
    output_gradient = shifted.astype(jnp.bfloat16)
    up_gradient = adapter_scale * lax.dot_general(
        hidden_state, output_gradient, (((0,), (0,)), ((), ())), preferred_element_type=jnp.float32
    )
    hidden_gradient = (
        adapter_scale
        * lax.dot_general(
            output_gradient,
            up_full,
            (((1,), (1,)), ((), ())),
            preferred_element_type=jnp.float32,
        )
    ).astype(jnp.bfloat16)
    down_grad = lax.dot_general(
        hidden_gradient, arrived, (((0,), (0,)), ((), ())), preferred_element_type=jnp.float32
    )

    both_grads = jnp.concatenate([down_grad, up_gradient], axis=0)
    summed = lax.psum_scatter(both_grads, "dp", scatter_dimension=1, tiled=True)
    down_share = summed[:rank]
    up_share = summed[rank:]
    down_update = adam_update(down_share, down_moment_first[0], down_moment_second[0])
    up_update = adam_update(up_share, up_moment_first[0], up_moment_second[0])

    returned_loss = lax.all_to_all(
        slot_loss.reshape(owner_count, slot_capacity),
        "owner",
        split_axis=0,
        concat_axis=0,
        tiled=True,
    ).reshape(slots)
    token_loss = jnp.take(returned_loss, target, axis=0)
    return (down_update[None], up_update[None], token_loss)


def solution(mesh):
    return jax.shard_map(
        body,
        mesh=mesh,
        in_specs=(
            P(("dp", "owner"), None),
            P(("dp", "owner"), None),
            P(("dp", "owner"), None),
            P("owner", None, "dp"),
            P("owner", None, "dp"),
            P("owner", None, "dp"),
            P("owner", None, "dp"),
            P("owner", None, "dp"),
            P("owner", None, "dp"),
        ),
        out_specs=(P("owner", None, "dp"), P("owner", None, "dp"), P(("dp", "owner"))),
        check_vma=False,
    )
```

```python
import jax
import jax.numpy as jnp
from jax import lax
from jax.sharding import PartitionSpec as P

adapter_scale = 0.5
adam_eps = 1e-08


def adam_update(grad, first, second):
    first_new = 0.9 * first.astype(jnp.float32) + 0.1 * grad
    second_new = 0.95 * second.astype(jnp.float32) + 0.05 * grad * grad
    return first_new / (jnp.sqrt(second_new) + adam_eps)


def step(
    tokens,
    residual,
    token_adapter_index,
    adapter_down_weight,
    adapter_up_weight,
    down_moment_first,
    down_moment_second,
    up_moment_first,
    up_moment_second,
):
    owner_count = lax.axis_size("owner")
    tok_rows = tokens.shape[0]
    width = tokens.shape[1]
    rank = adapter_down_weight.shape[1]
    slot_capacity = max(2, 3 * tok_rows // (2 * owner_count))
    slots = owner_count * slot_capacity
    route_ids = token_adapter_index[:, 0]
    member = (route_ids[:, None] == jnp.arange(owner_count, dtype=jnp.int32)[None, :]).astype(
        jnp.int32
    )
    before = jnp.cumsum(member, axis=0) - member
    within = jnp.sum(before * member, axis=1)
    target = route_ids * slot_capacity + within
    dispatch = (jnp.arange(slots, dtype=jnp.int32)[:, None] == target[None, :]).astype(
        jnp.bfloat16
    )

    pieces = lax.axis_size("dp")
    piece = width // pieces
    valid = jnp.sum(dispatch, axis=1) > 0
    source = jnp.argmax(dispatch, axis=1)

    both_weights = jnp.concatenate([adapter_down_weight[0], adapter_up_weight[0]], axis=0)
    both_full = lax.all_gather(both_weights, "dp", axis=1, tiled=True)
    down_full = both_full[:rank]
    up_full = both_full[rank:]

    def place(row_block):
        split_rows = row_block.reshape(tok_rows, pieces, piece)
        picked = jnp.where(valid[:, None, None], split_rows[source], jnp.zeros((), row_block.dtype))
        return picked.reshape(owner_count, slot_capacity * pieces, piece)

    def send(row_block):
        return lax.all_to_all(row_block, "owner", split_axis=0, concat_axis=0, tiled=True)

    placed_tokens = place(tokens)
    arrived_tokens = send(placed_tokens)
    placed_residual, arrived_tokens = lax.optimization_barrier((place(residual), arrived_tokens))
    arrived = arrived_tokens.reshape(slots, width)
    arrived_residual = lax.all_to_all(
        placed_residual, "owner", split_axis=0, concat_axis=0, tiled=True
    )
    arrived_residual = lax.optimization_barrier(arrived_residual.reshape(slots, width))

    hidden_state = lax.dot_general(
        arrived, down_full, (((1,), (1,)), ((), ())), preferred_element_type=jnp.float32
    ).astype(jnp.bfloat16)
    adapter_output = (
        adapter_scale * jnp.dot(hidden_state, up_full, preferred_element_type=jnp.float32)
    ).astype(jnp.bfloat16)
    shifted = arrived_residual.astype(jnp.float32) + adapter_output.astype(jnp.float32)
    slot_loss = jnp.mean(0.5 * shifted * shifted, axis=1)
    output_gradient = shifted.astype(jnp.bfloat16)
    up_gradient = adapter_scale * lax.dot_general(
        hidden_state, output_gradient, (((0,), (0,)), ((), ())), preferred_element_type=jnp.float32
    )
    hidden_gradient = (
        adapter_scale
        * lax.dot_general(
            output_gradient,
            up_full,
            (((1,), (1,)), ((), ())),
            preferred_element_type=jnp.float32,
        )
    ).astype(jnp.bfloat16)
    down_grad = lax.dot_general(
        hidden_gradient, arrived, (((0,), (0,)), ((), ())), preferred_element_type=jnp.float32
    )

    both_grads = jnp.concatenate([down_grad, up_gradient], axis=0)
    summed = lax.psum_scatter(both_grads, "dp", scatter_dimension=1, tiled=True)
    down_share = summed[:rank]
    up_share = summed[rank:]
    down_update = adam_update(down_share, down_moment_first[0], down_moment_second[0])
    up_update = adam_update(up_share, up_moment_first[0], up_moment_second[0])

    returned_loss = lax.all_to_all(
        slot_loss.reshape(owner_count, slot_capacity),
        "owner",
        split_axis=0,
        concat_axis=0,
        tiled=True,
    ).reshape(slots)
    token_loss = jnp.take(returned_loss, target, axis=0)
    return (down_update[None], up_update[None], token_loss)


def solution(mesh):
    return jax.shard_map(
        step,
        mesh=mesh,
        in_specs=(
            P(("dp", "owner"), None),
            P(("dp", "owner"), None),
            P(("dp", "owner"), None),
            P("owner", None, "dp"),
            P("owner", None, "dp"),
            P("owner", None, "dp"),
            P("owner", None, "dp"),
            P("owner", None, "dp"),
            P("owner", None, "dp"),
        ),
        out_specs=(P("owner", None, "dp"), P("owner", None, "dp"), P(("dp", "owner"))),
        check_vma=False,
    )
```

```python
import jax
import jax.numpy as jnp
from jax import lax
from jax.sharding import PartitionSpec as P

adapter_scale = 0.5
adam_eps = 1e-08


def adam_update(grad, first, second):
    first_new = 0.9 * first.astype(jnp.float32) + 0.1 * grad
    second_new = 0.95 * second.astype(jnp.float32) + 0.05 * grad * grad
    return first_new / (jnp.sqrt(second_new) + adam_eps)


def step(
    tokens,
    residual,
    token_adapter_index,
    adapter_down_weight,
    adapter_up_weight,
    down_moment_first,
    down_moment_second,
    up_moment_first,
    up_moment_second,
):
    owner_count = lax.axis_size("owner")
    tok_rows = tokens.shape[0]
    width = tokens.shape[1]
    rank = adapter_down_weight.shape[1]
    slot_capacity = max(2, 3 * tok_rows // (2 * owner_count))
    slots = owner_count * slot_capacity
    route_ids = token_adapter_index[:, 0]
    member = (route_ids[:, None] == jnp.arange(owner_count, dtype=jnp.int32)[None, :]).astype(
        jnp.int32
    )
    before = jnp.cumsum(member, axis=0) - member
    within = jnp.sum(before * member, axis=1)
    target = route_ids * slot_capacity + within
    dispatch = (jnp.arange(slots, dtype=jnp.int32)[:, None] == target[None, :]).astype(
        jnp.bfloat16
    )

    pieces = lax.axis_size("dp")
    piece = width // pieces
    valid = jnp.sum(dispatch, axis=1) > 0
    source = jnp.argmax(dispatch, axis=1)

    both_weights = jnp.concatenate([adapter_down_weight[0], adapter_up_weight[0]], axis=0)
    both_full = lax.all_gather(both_weights, "dp", axis=1, tiled=True)
    down_full = both_full[:rank]
    up_full = both_full[rank:]

    def place(row_block):
        split_rows = row_block.reshape(tok_rows, pieces, piece)
        picked = jnp.where(valid[:, None, None], split_rows[source], jnp.zeros((), row_block.dtype))
        return picked.reshape(owner_count, slot_capacity * pieces, piece)

    def send(row_block):
        return lax.all_to_all(row_block, "owner", split_axis=0, concat_axis=0, tiled=True)

    placed = jnp.concatenate([place(tokens), place(residual)], axis=1)
    arrived_both = send(placed)
    half = slot_capacity * pieces
    arrived = lax.optimization_barrier(arrived_both[:, :half].reshape(slots, width))
    arrived_residual = lax.optimization_barrier(arrived_both[:, half:].reshape(slots, width))

    hidden_state = lax.dot_general(
        arrived, down_full, (((1,), (1,)), ((), ())), preferred_element_type=jnp.float32
    ).astype(jnp.bfloat16)
    adapter_output = (
        adapter_scale * jnp.dot(hidden_state, up_full, preferred_element_type=jnp.float32)
    ).astype(jnp.bfloat16)
    shifted = arrived_residual.astype(jnp.float32) + adapter_output.astype(jnp.float32)
    slot_loss = jnp.mean(0.5 * shifted * shifted, axis=1)
    output_gradient = shifted.astype(jnp.bfloat16)
    up_gradient = adapter_scale * lax.dot_general(
        hidden_state, output_gradient, (((0,), (0,)), ((), ())), preferred_element_type=jnp.float32
    )
    hidden_gradient = (
        adapter_scale
        * lax.dot_general(
            output_gradient,
            up_full,
            (((1,), (1,)), ((), ())),
            preferred_element_type=jnp.float32,
        )
    ).astype(jnp.bfloat16)
    down_grad = lax.dot_general(
        hidden_gradient, arrived, (((0,), (0,)), ((), ())), preferred_element_type=jnp.float32
    )

    both_grads = jnp.concatenate([down_grad, up_gradient], axis=0)
    summed = lax.psum_scatter(both_grads, "dp", scatter_dimension=1, tiled=True)
    down_share = summed[:rank]
    up_share = summed[rank:]
    down_update = adam_update(down_share, down_moment_first[0], down_moment_second[0])
    up_update = adam_update(up_share, up_moment_first[0], up_moment_second[0])

    returned_loss = lax.all_to_all(
        slot_loss.reshape(owner_count, slot_capacity),
        "owner",
        split_axis=0,
        concat_axis=0,
        tiled=True,
    ).reshape(slots)
    token_loss = jnp.take(returned_loss, target, axis=0)
    return (down_update[None], up_update[None], token_loss)


def solution(mesh):
    return jax.shard_map(
        step,
        mesh=mesh,
        in_specs=(
            P(("dp", "owner"), None),
            P(("dp", "owner"), None),
            P(("dp", "owner"), None),
            P("owner", None, "dp"),
            P("owner", None, "dp"),
            P("owner", None, "dp"),
            P("owner", None, "dp"),
            P("owner", None, "dp"),
            P("owner", None, "dp"),
        ),
        out_specs=(P("owner", None, "dp"), P("owner", None, "dp"), P(("dp", "owner"))),
        check_vma=False,
    )
```

```python
import jax
import jax.numpy as jnp
from jax import lax
from jax.sharding import PartitionSpec as P

adapter_scale = 0.5
adam_eps = 1e-08


def adam_update(grad, first, second):
    first_new = 0.9 * first.astype(jnp.float32) + 0.1 * grad
    second_new = 0.95 * second.astype(jnp.float32) + 0.05 * grad * grad
    return first_new / (jnp.sqrt(second_new) + adam_eps)


def step(
    tokens,
    residual,
    token_adapter_index,
    adapter_down_weight,
    adapter_up_weight,
    down_moment_first,
    down_moment_second,
    up_moment_first,
    up_moment_second,
):
    owner_count = lax.axis_size("owner")
    tok_rows = tokens.shape[0]
    width = tokens.shape[1]
    rank = adapter_down_weight.shape[1]
    slot_capacity = max(2, 3 * tok_rows // (2 * owner_count))
    slots = owner_count * slot_capacity
    route_ids = token_adapter_index[:, 0]
    member = (route_ids[:, None] == jnp.arange(owner_count, dtype=jnp.int32)[None, :]).astype(
        jnp.int32
    )
    before = jnp.cumsum(member, axis=0) - member
    within = jnp.sum(before * member, axis=1)
    target = route_ids * slot_capacity + within
    dispatch = (jnp.arange(slots, dtype=jnp.int32)[:, None] == target[None, :]).astype(
        jnp.bfloat16
    )

    pieces = lax.axis_size("dp")
    piece = width // pieces
    valid = jnp.sum(dispatch, axis=1) > 0
    source = jnp.argmax(dispatch, axis=1)

    both_weights = jnp.concatenate([adapter_down_weight[0], adapter_up_weight[0]], axis=0)
    both_full = lax.all_gather(both_weights, "dp", axis=1, tiled=True)
    down_full = both_full[:rank]
    up_full = both_full[rank:]

    def place(row_block):
        split_rows = row_block.reshape(tok_rows, pieces, piece)
        picked = jnp.where(valid[:, None, None], split_rows[source], jnp.zeros((), row_block.dtype))
        return picked.reshape(owner_count, slot_capacity * pieces, piece)

    def send(row_block):
        return lax.all_to_all(row_block, "owner", split_axis=0, concat_axis=0, tiled=True)

    placed = jnp.concatenate([place(tokens), place(residual)], axis=1)
    arrived_both = send(placed)
    both_rows = lax.optimization_barrier(
        arrived_both.reshape(owner_count, 2, slot_capacity, pieces, piece)
        .transpose(1, 0, 2, 3, 4)
        .reshape(2, slots, width)
    )
    arrived = both_rows[0]
    arrived_residual = both_rows[1]

    hidden_state = lax.dot_general(
        arrived, down_full, (((1,), (1,)), ((), ())), preferred_element_type=jnp.float32
    ).astype(jnp.bfloat16)
    adapter_output = (
        adapter_scale * jnp.dot(hidden_state, up_full, preferred_element_type=jnp.float32)
    ).astype(jnp.bfloat16)
    shifted = arrived_residual.astype(jnp.float32) + adapter_output.astype(jnp.float32)
    slot_loss = jnp.mean(0.5 * shifted * shifted, axis=1)
    output_gradient = shifted.astype(jnp.bfloat16)
    up_gradient = adapter_scale * lax.dot_general(
        hidden_state, output_gradient, (((0,), (0,)), ((), ())), preferred_element_type=jnp.float32
    )
    hidden_gradient = (
        adapter_scale
        * lax.dot_general(
            output_gradient,
            up_full,
            (((1,), (1,)), ((), ())),
            preferred_element_type=jnp.float32,
        )
    ).astype(jnp.bfloat16)
    down_grad = lax.dot_general(
        hidden_gradient, arrived, (((0,), (0,)), ((), ())), preferred_element_type=jnp.float32
    )

    both_grads = jnp.concatenate([down_grad, up_gradient], axis=0)
    summed = lax.psum_scatter(both_grads, "dp", scatter_dimension=1, tiled=True)
    down_share = summed[:rank]
    up_share = summed[rank:]
    down_update = adam_update(down_share, down_moment_first[0], down_moment_second[0])
    up_update = adam_update(up_share, up_moment_first[0], up_moment_second[0])

    returned_loss = lax.all_to_all(
        slot_loss.reshape(owner_count, slot_capacity),
        "owner",
        split_axis=0,
        concat_axis=0,
        tiled=True,
    ).reshape(slots)
    token_loss = jnp.take(returned_loss, target, axis=0)
    return (down_update[None], up_update[None], token_loss)


def solution(mesh):
    return jax.shard_map(
        step,
        mesh=mesh,
        in_specs=(
            P(("dp", "owner"), None),
            P(("dp", "owner"), None),
            P(("dp", "owner"), None),
            P("owner", None, "dp"),
            P("owner", None, "dp"),
            P("owner", None, "dp"),
            P("owner", None, "dp"),
            P("owner", None, "dp"),
            P("owner", None, "dp"),
        ),
        out_specs=(P("owner", None, "dp"), P("owner", None, "dp"), P(("dp", "owner"))),
        check_vma=False,
    )
```

```python
import jax
import jax.numpy as jnp
from jax import lax
from jax.sharding import PartitionSpec as P

adapter_scale = 0.5
adam_eps = 1e-08


def adam_update(grad, first, second):
    first_new = 0.9 * first.astype(jnp.float32) + 0.1 * grad
    second_new = 0.95 * second.astype(jnp.float32) + 0.05 * grad * grad
    return first_new / (jnp.sqrt(second_new) + adam_eps)


def step(
    tokens,
    residual,
    token_adapter_index,
    adapter_down_weight,
    adapter_up_weight,
    down_moment_first,
    down_moment_second,
    up_moment_first,
    up_moment_second,
):
    owner_count = lax.axis_size("owner")
    tok_rows = tokens.shape[0]
    width = tokens.shape[1]
    rank = adapter_down_weight.shape[1]
    slot_capacity = max(2, 3 * tok_rows // (2 * owner_count))
    slots = owner_count * slot_capacity
    route_ids = token_adapter_index[:, 0]
    member = (route_ids[:, None] == jnp.arange(owner_count, dtype=jnp.int32)[None, :]).astype(
        jnp.int32
    )
    before = jnp.cumsum(member, axis=0) - member
    within = jnp.sum(before * member, axis=1)
    target = route_ids * slot_capacity + within
    dispatch = (jnp.arange(slots, dtype=jnp.int32)[:, None] == target[None, :]).astype(
        jnp.bfloat16
    )

    pieces = lax.axis_size("dp")
    piece = width // pieces
    valid = jnp.sum(dispatch, axis=1) > 0
    source = jnp.argmax(dispatch, axis=1)

    both_weights = jnp.concatenate([adapter_down_weight[0], adapter_up_weight[0]], axis=0)
    both_full = lax.all_gather(both_weights, "dp", axis=1, tiled=True)
    down_full = both_full[:rank]
    up_full = both_full[rank:]

    def place(row_block):
        split_rows = row_block.reshape(tok_rows, pieces, piece)
        picked = jnp.where(valid[:, None, None], split_rows[source], jnp.zeros((), row_block.dtype))
        return picked.reshape(owner_count, slot_capacity * pieces, piece)

    def send(row_block):
        return lax.all_to_all(row_block, "owner", split_axis=0, concat_axis=0, tiled=True)

    placed = jnp.concatenate([place(tokens), place(residual)], axis=1)
    arrived_both = send(placed)
    both_rows = lax.optimization_barrier(
        arrived_both.reshape(owner_count, 2, slot_capacity, pieces, piece)
        .transpose(1, 0, 2, 3, 4)
        .reshape(2, slots, width)
    )
    arrived = both_rows[0]
    arrived_residual = both_rows[1]

    hidden_state = lax.dot_general(
        arrived, down_full, (((1,), (1,)), ((), ())), preferred_element_type=jnp.float32
    ).astype(jnp.bfloat16)
    adapter_output = (
        adapter_scale * jnp.dot(hidden_state, up_full, preferred_element_type=jnp.float32)
    ).astype(jnp.bfloat16)
    shifted = arrived_residual.astype(jnp.float32) + adapter_output.astype(jnp.float32)
    slot_loss = jnp.mean(0.5 * shifted * shifted, axis=1)
    output_gradient = shifted.astype(jnp.bfloat16)
    hidden_gradient = (
        adapter_scale
        * lax.dot_general(
            output_gradient,
            up_full,
            (((1,), (1,)), ((), ())),
            preferred_element_type=jnp.float32,
        )
    ).astype(jnp.bfloat16)

    right = both_rows.at[1].set(output_gradient)
    left = jnp.stack([hidden_gradient, hidden_state])
    both_grads = lax.dot_general(
        left, right, (((1,), (1,)), ((0,), (0,))), preferred_element_type=jnp.float32
    )
    both_grads = both_grads * jnp.array([1.0, adapter_scale], jnp.float32)[:, None, None]
    both_grads = both_grads.reshape(2 * rank, width)

    summed = lax.psum_scatter(both_grads, "dp", scatter_dimension=1, tiled=True)
    down_share = summed[:rank]
    up_share = summed[rank:]
    down_update = adam_update(down_share, down_moment_first[0], down_moment_second[0])
    up_update = adam_update(up_share, up_moment_first[0], up_moment_second[0])

    returned_loss = lax.all_to_all(
        slot_loss.reshape(owner_count, slot_capacity),
        "owner",
        split_axis=0,
        concat_axis=0,
        tiled=True,
    ).reshape(slots)
    token_loss = jnp.take(returned_loss, target, axis=0)
    return (down_update[None], up_update[None], token_loss)


def solution(mesh):
    return jax.shard_map(
        step,
        mesh=mesh,
        in_specs=(
            P(("dp", "owner"), None),
            P(("dp", "owner"), None),
            P(("dp", "owner"), None),
            P("owner", None, "dp"),
            P("owner", None, "dp"),
            P("owner", None, "dp"),
            P("owner", None, "dp"),
            P("owner", None, "dp"),
            P("owner", None, "dp"),
        ),
        out_specs=(P("owner", None, "dp"), P("owner", None, "dp"), P(("dp", "owner"))),
        check_vma=False,
    )
```
